256 devices in a mesh: band: 16 (over x, y_lo, core), dom: 16 (over z, y_hi).
Axes of the slice: x: 4, y: 4 (y_hi: 2, y_lo: 2; y = y_hi * 2 + y_lo), z: 8, core: 2. Of those that a mesh axis runs over, the one named last changes fastest.
Arguments:
- psi: float32 [1024, 64, 8, 128], P('band', 'dom'), may hold values from -6 to 6
- potential: float32 [64, 8, 128], P('dom'), may hold values from -1 to 1
- owner: int32 [1], replicated, may hold values from 0 to 15
Outputs:
- filtered: float32 [1024, 64, 8, 128], P('band', 'dom')
- intersection: float32 [64, 1024], P(None, 'band')
- hamiltonian: float32 [64, 1024], P(None, 'band')
The draws below stay inside these ranges and needn't reach their ends.
Inputs may be any that keep to these rules, and one draw needn't show every extreme that they name: The owner's panel holds bands 64 * owner to 64 * owner + 63.
All inputs are finite; a program needn't handle non-finite values.
Results may differ from the reference program's by a relative error of at most 0.000084.
Values sent between devices are 32-bit elements; how exact they have to be, the bound alone decides.
No kernel may reach another device: no remote copies, remote signals or barrier semaphores. Data moves between devices by JAX's collectives and lax.ppermute only.
A program may use at most 64 MiB of HBM per device.

```python
import jax
import jax.numpy as jnp
from jax import lax

OWN = 64
NY = 8
NZ = 128
BANDS = 1024
NX = 64
N_BAND = 16


def level_of(stream_key, extent, cuts, low, high):
    def one(position, shards_of):
        steps = jax.random.uniform(jax.random.fold_in(jax.random.fold_in(stream_key, 6), position), (shards_of,), jnp.float32, low / len(cuts), high / len(cuts))
        return jnp.repeat(jnp.exp(steps), extent[position] // shards_of).reshape((-1,) + (1,) * (len(extent) - position - 1))

    loudness = one(*cuts[0])
    for cut in cuts[1:]:
        loudness = loudness * one(*cut)
    return loudness


def scatter_about(rng, extent, scale, limit, split=(), held_as=jnp.bfloat16):
    drawn = scale * jax.random.normal(rng, extent, jnp.float32)
    if split:
        drawn = drawn * level_of(rng, extent, split, -0.22, 0.18)
    return jnp.clip(drawn, -limit, limit).astype(held_as)


def setup_inputs(seed: int = 0) -> dict:
    arg_keys = jax.random.split(jax.random.key(seed), 4)
    psi = scatter_about(arg_keys[0], (BANDS, NX, NY, NZ), 1.0, 6.0, ((0, 16), (1, 16)), jnp.float32)
    potential = jnp.clip(jax.random.uniform(arg_keys[1], (NX, NY, NZ), jnp.float32, -1.0, 1.0) * level_of(arg_keys[1], (NX, NY, NZ), ((0, 16),), -0.4, 0.0), -1.0, 1.0)
    owner = jax.random.randint(arg_keys[2], (1,), 0, BANDS // OWN).astype(jnp.int32)
    return {"psi": psi, "potential": potential, "owner": owner}


center = 4.9
halfwidth = 4.1


def lap_periodic(grid_field, which_axis):
    outer = jnp.roll(grid_field, 2, which_axis) + jnp.roll(grid_field, -2, which_axis)
    nearer = jnp.roll(grid_field, 1, which_axis) + jnp.roll(grid_field, -1, which_axis)
    return (-1.0 / 12.0) * outer + (4.0 / 3.0) * nearer - 2.5 * grid_field


def hamiltonian_apply(extended, local_potential):
    interior = extended[:, 2:-2]
    along_first = (-1.0 / 12.0) * (extended[:, :-4] + extended[:, 4:]) + (4.0 / 3.0) * (extended[:, 1:-3] + extended[:, 3:-1]) - 2.5 * interior
    laplace = along_first + lap_periodic(interior, 2) + lap_periodic(interior, 3)
    return -0.5 * laplace + local_potential * interior


def shifted(extended, local_potential):
    return (hamiltonian_apply(extended, local_potential) - center * extended[:, 2:-2]) / halfwidth


def extend(grid_field):
    return jnp.concatenate([grid_field[:, -2:], grid_field, grid_field[:, :2]], axis=1)


def cheb_filter(band_block, potential):
    first_term = shifted(extend(band_block), potential)
    return 2.0 * shifted(extend(first_term), potential) - band_block


def reference(psi, potential, owner):
    start = (owner[0] * OWN).astype(jnp.int32)
    owned_start = lax.dynamic_slice_in_dim(psi, start, OWN, 0)
    owned_panel = cheb_filter(owned_start, potential)
    applied = hamiltonian_apply(extend(owned_panel), potential)
    scale = 1.0 / (NX * NY * NZ)
    panel_flat = owned_panel.reshape(OWN, -1)
    applied_flat = applied.reshape(OWN, -1)
    blocks = psi.reshape(N_BAND, OWN, NX, NY, NZ)

    def per_block(band_block):
        result = cheb_filter(band_block, potential)
        flattened = result.reshape(OWN, -1)
        over_rows = jnp.einsum("pc,bc->pb", panel_flat, flattened, precision=lax.Precision.HIGHEST) * scale
        ham_rows = jnp.einsum("pc,bc->pb", applied_flat, flattened, precision=lax.Precision.HIGHEST) * scale
        return result, over_rows, ham_rows

    results, over_all, ham_all = lax.map(per_block, blocks)
    filtered = results.reshape(psi.shape)
    intersection = jnp.transpose(over_all, (1, 0, 2)).reshape(OWN, -1)
    hamiltonian = jnp.transpose(ham_all, (1, 0, 2)).reshape(OWN, -1)
    return filtered, intersection, hamiltonian
```

```python
import jax
import jax.numpy as jnp
from jax import lax
from jax.sharding import PartitionSpec as P

center = 4.9
halfwidth = 4.1


def extended_2(block, sides, width):
    for axis, dim in sides:
        count = lax.axis_size(axis)
        forward = [(i, i + 1) for i in range(count - 1)]
        forward.append((count - 1, 0))
        backward = [(target, source) for source, target in forward]
        low = lax.ppermute(
            lax.slice_in_dim(block, block.shape[dim] - width, None, axis=dim), axis, forward
        )
        high = lax.ppermute(lax.slice_in_dim(block, 0, width, axis=dim), axis, backward)
        block = jnp.concatenate([low, block, high], axis=dim)
    return block


def broadcast(array, axis, root):
    count = lax.axis_size(axis)
    piece = array.shape[0] // count
    spread = lax.all_to_all(array, axis, 0, 0, tiled=True)
    mine = lax.dynamic_slice_in_dim(spread, root * piece, piece, 0)
    return lax.all_gather(mine, axis, axis=0, tiled=True)


def doubling_sum(array, axis):
    count = lax.axis_size(axis)
    step = 1
    while step < count:
        array = array + lax.ppermute(array, axis, [(i, i ^ step) for i in range(count)])
        step *= 2
    return array


def lap_periodic(grid_field, which_axis):
    outer = jnp.roll(grid_field, 2, which_axis) + jnp.roll(grid_field, -2, which_axis)
    nearer = jnp.roll(grid_field, 1, which_axis) + jnp.roll(grid_field, -1, which_axis)
    return -1.0 / 12.0 * outer + 4.0 / 3.0 * nearer - 2.5 * grid_field


def hamiltonian_apply(extended, local_potential):
    interior = extended[:, 2:-2]
    along_first = (
        -1.0 / 12.0 * (extended[:, :-4] + extended[:, 4:])
        + 4.0 / 3.0 * (extended[:, 1:-3] + extended[:, 3:-1])
        - 2.5 * interior
    )
    laplace = along_first + lap_periodic(interior, 2) + lap_periodic(interior, 3)
    return -0.5 * laplace + local_potential * interior


def shifted(extended, local_potential):
    return (hamiltonian_apply(extended, local_potential) - center * extended[:, 2:-2]) / halfwidth


def with_faces(grid_field):
    return extended_2(grid_field, (("dom", 1),), 2)


def body(psi, potential, owner):
    current = psi
    first_term = shifted(with_faces(current), potential)
    current = 2.0 * shifted(with_faces(first_term), potential) - current
    local_bands = current.shape[0]
    owner_root = owner[0]
    owned_panel = broadcast(current, "band", owner_root)
    total_cells = current.shape[1] * current.shape[2] * current.shape[3] * lax.axis_size("dom")
    scale = 1.0 / total_cells
    flattened = current.reshape(local_bands, -1)
    panel_flat = owned_panel.reshape(local_bands, -1)
    extended = extended_2(current, (("dom", 1),), 2)
    applied = hamiltonian_apply(extended, potential)
    ham_rows = jnp.einsum(
        "pc,bc->pb", panel_flat, applied.reshape(local_bands, -1), precision=lax.Precision.HIGHEST
    )
    over_rows = jnp.einsum("pc,bc->pb", panel_flat, flattened, precision=lax.Precision.HIGHEST)
    both = doubling_sum(jnp.stack([over_rows * scale, ham_rows * scale]), "dom")
    return (current, both[0], both[1])


def solution(mesh):
    placed = (P("band", "dom", None, None), P("dom", None, None), P())
    return jax.shard_map(
        body,
        mesh=mesh,
        in_specs=placed,
        out_specs=(P("band", "dom", None, None), P(None, "band"), P(None, "band")),
        check_vma=False,
    )
```

```python
import jax
import jax.numpy as jnp
from jax import lax
from jax.sharding import PartitionSpec as P

center = 4.9
halfwidth = 4.1


def extended_2(block, sides, width):
    for axis, dim in sides:
        count = lax.axis_size(axis)
        forward = [(i, i + 1) for i in range(count - 1)]
        forward.append((count - 1, 0))
        backward = [(target, source) for source, target in forward]
        low = lax.ppermute(
            lax.slice_in_dim(block, block.shape[dim] - width, None, axis=dim), axis, forward
        )
        high = lax.ppermute(lax.slice_in_dim(block, 0, width, axis=dim), axis, backward)
        block = jnp.concatenate([low, block, high], axis=dim)
    return block


def broadcast(array, axis, root):
    count = lax.axis_size(axis)
    piece = array.shape[0] // count
    spread = lax.all_to_all(array, axis, 0, 0, tiled=True)
    mine = lax.dynamic_slice_in_dim(spread, root * piece, piece, 0)
    return lax.all_to_all(jnp.concatenate([mine] * count, 0), axis, 0, 0, tiled=True)


def doubling_sum(array, axis):
    count = lax.axis_size(axis)
    step = 1
    while step < count:
        array = array + lax.ppermute(array, axis, [(i, i ^ step) for i in range(count)])
        step *= 2
    return array


def lap_periodic(grid_field, which_axis):
    outer = jnp.roll(grid_field, 2, which_axis) + jnp.roll(grid_field, -2, which_axis)
    nearer = jnp.roll(grid_field, 1, which_axis) + jnp.roll(grid_field, -1, which_axis)
    return -1.0 / 12.0 * outer + 4.0 / 3.0 * nearer - 2.5 * grid_field


def hamiltonian_apply(extended, local_potential):
    interior = extended[:, 2:-2]
    along_first = (
        -1.0 / 12.0 * (extended[:, :-4] + extended[:, 4:])
        + 4.0 / 3.0 * (extended[:, 1:-3] + extended[:, 3:-1])
        - 2.5 * interior
    )
    laplace = along_first + lap_periodic(interior, 2) + lap_periodic(interior, 3)
    return -0.5 * laplace + local_potential * interior


def shifted(extended, local_potential):
    return (hamiltonian_apply(extended, local_potential) - center * extended[:, 2:-2]) / halfwidth


def with_faces(grid_field):
    return extended_2(grid_field, (("dom", 1),), 2)


def body(psi, potential, owner):
    current = psi
    first_term = shifted(with_faces(current), potential)
    current = 2.0 * shifted(with_faces(first_term), potential) - current
    local_bands = current.shape[0]
    owner_root = owner[0]
    owned_panel = broadcast(current, "band", owner_root)
    total_cells = current.shape[1] * current.shape[2] * current.shape[3] * lax.axis_size("dom")
    scale = 1.0 / total_cells
    flattened = current.reshape(local_bands, -1)
    panel_flat = owned_panel.reshape(local_bands, -1)
    extended = extended_2(current, (("dom", 1),), 2)
    applied = hamiltonian_apply(extended, potential)
    ham_rows = jnp.einsum(
        "pc,bc->pb", panel_flat, applied.reshape(local_bands, -1), precision=lax.Precision.HIGHEST
    )
    over_rows = jnp.einsum("pc,bc->pb", panel_flat, flattened, precision=lax.Precision.HIGHEST)
    both = doubling_sum(jnp.stack([over_rows * scale, ham_rows * scale]), "dom")
    return (current, both[0], both[1])


def solution(mesh):
    placed = (P("band", "dom", None, None), P("dom", None, None), P())
    return jax.shard_map(
        body,
        mesh=mesh,
        in_specs=placed,
        out_specs=(P("band", "dom", None, None), P(None, "band"), P(None, "band")),
        check_vma=False,
    )
```

```python
import jax
import jax.numpy as jnp
from jax import lax
from jax.sharding import PartitionSpec as P

center = 4.9
halfwidth = 4.1


def broadcast(array, axis, root):
    count = lax.axis_size(axis)
    piece = array.shape[0] // count
    spread = lax.all_to_all(array, axis, 0, 0, tiled=True)
    mine = lax.dynamic_slice_in_dim(spread, root * piece, piece, 0)
    return lax.all_to_all(jnp.concatenate([mine] * count, 0), axis, 0, 0, tiled=True)


def doubling_sum(array, axis):
    count = lax.axis_size(axis)
    step = 1
    while step < count:
        array = array + lax.ppermute(array, axis, [(i, i ^ step) for i in range(count)])
        step *= 2
    return array


def lap_periodic(grid_field, which_axis):
    outer = jnp.roll(grid_field, 2, which_axis) + jnp.roll(grid_field, -2, which_axis)
    nearer = jnp.roll(grid_field, 1, which_axis) + jnp.roll(grid_field, -1, which_axis)
    return -1.0 / 12.0 * outer + 4.0 / 3.0 * nearer - 2.5 * grid_field


def hamiltonian_apply(extended, local_potential):
    interior = extended[:, 2:-2]
    along_first = (
        -1.0 / 12.0 * (extended[:, :-4] + extended[:, 4:])
        + 4.0 / 3.0 * (extended[:, 1:-3] + extended[:, 3:-1])
        - 2.5 * interior
    )
    laplace = along_first + lap_periodic(interior, 2) + lap_periodic(interior, 3)
    return -0.5 * laplace + local_potential * interior


def shifted(extended, local_potential):
    return (hamiltonian_apply(extended, local_potential) - center * extended[:, 2:-2]) / halfwidth


def shifted_to(block, axis, shift):
    count = lax.axis_size(axis)
    return lax.ppermute(block, axis, [(i, (i + shift) % count) for i in range(count)])


def with_faces(block, dim, axis, width):
    n = block.shape[dim]
    low, high = [], []
    for hop in range(1, -(-width // n) + 1):
        take = min(n, width - n * (hop - 1))
        low.insert(0, shifted_to(lax.slice_in_dim(block, n - take, None, axis=dim), axis, hop))
        high.append(shifted_to(lax.slice_in_dim(block, 0, take, axis=dim), axis, -hop))
    return jnp.concatenate(low + [block] + high, axis=dim)


def body(psi, potential, owner):
    wide = with_faces(psi, 1, "dom", 6)
    pot_wide = with_faces(potential, 0, "dom", 4)
    first_term = shifted(wide, pot_wide)
    filtered_wide = 2.0 * shifted(first_term, pot_wide[2:-2]) - wide[:, 4:-4]
    current = filtered_wide[:, 2:-2]
    local_bands = current.shape[0]
    owner_root = owner[0]
    owned_panel = broadcast(current, "band", owner_root)
    total_cells = current.shape[1] * current.shape[2] * current.shape[3] * lax.axis_size("dom")
    scale = 1.0 / total_cells
    flattened = current.reshape(local_bands, -1)
    panel_flat = owned_panel.reshape(local_bands, -1)
    applied = hamiltonian_apply(filtered_wide, potential)
    ham_rows = jnp.einsum(
        "pc,bc->pb", panel_flat, applied.reshape(local_bands, -1), precision=lax.Precision.HIGHEST
    )
    over_rows = jnp.einsum("pc,bc->pb", panel_flat, flattened, precision=lax.Precision.HIGHEST)
    both = doubling_sum(jnp.stack([over_rows * scale, ham_rows * scale]), "dom")
    return (current, both[0], both[1])


def solution(mesh):
    placed = (P("band", "dom", None, None), P("dom", None, None), P())
    return jax.shard_map(
        body,
        mesh=mesh,
        in_specs=placed,
        out_specs=(P("band", "dom", None, None), P(None, "band"), P(None, "band")),
        check_vma=False,
    )
```

```python
import jax
import jax.numpy as jnp
from jax import lax
from jax.experimental import pallas as pl
from jax.experimental.pallas import tpu as pltpu
from jax.sharding import PartitionSpec as P


center = 4.9
halfwidth = 4.1


def broadcast(array, axis, root):
    count = lax.axis_size(axis)
    piece = array.shape[0] // count
    spread = lax.all_to_all(array, axis, 0, 0, tiled=True)
    mine = lax.dynamic_slice_in_dim(spread, root * piece, piece, 0)
    return lax.all_to_all(jnp.concatenate([mine] * count, 0), axis, 0, 0, tiled=True)


def doubling_sum(array, axis):
    count = lax.axis_size(axis)
    step = 1
    while step < count:
        array = array + lax.ppermute(array, axis, [(i, i ^ step) for i in range(count)])
        step *= 2
    return array


def lap_periodic(grid_field, which_axis):
    outer = jnp.roll(grid_field, 2, which_axis) + jnp.roll(grid_field, -2, which_axis)
    nearer = jnp.roll(grid_field, 1, which_axis) + jnp.roll(grid_field, -1, which_axis)
    return -1.0 / 12.0 * outer + 4.0 / 3.0 * nearer - 2.5 * grid_field


def hamiltonian_apply(extended, local_potential):
    interior = extended[:, 2:-2]
    along_first = (
        -1.0 / 12.0 * (extended[:, :-4] + extended[:, 4:])
        + 4.0 / 3.0 * (extended[:, 1:-3] + extended[:, 3:-1])
        - 2.5 * interior
    )
    laplace = along_first + lap_periodic(interior, 2) + lap_periodic(interior, 3)
    return -0.5 * laplace + local_potential * interior


def shifted(extended, local_potential):
    return (hamiltonian_apply(extended, local_potential) - center * extended[:, 2:-2]) / halfwidth


def shifted_to(block, axis, shift):
    count = lax.axis_size(axis)
    return lax.ppermute(block, axis, [(i, (i + shift) % count) for i in range(count)])


def face_pieces(block, dim, axis, width):
    n = block.shape[dim]
    low, high = [], []
    for hop in range(1, -(-width // n) + 1):
        take = min(n, width - n * (hop - 1))
        low.insert(0, shifted_to(lax.slice_in_dim(block, n - take, None, axis=dim), axis, hop))
        high.append(shifted_to(lax.slice_in_dim(block, 0, take, axis=dim), axis, -hop))
    return low + [block] + high


def kernel_lap(field, which_axis):
    size = field.shape[which_axis]
    outer = pltpu.roll(field, 2, which_axis) + pltpu.roll(field, size - 2, which_axis)
    nearer = pltpu.roll(field, 1, which_axis) + pltpu.roll(field, size - 1, which_axis)
    return -1.0 / 12.0 * outer + 4.0 / 3.0 * nearer - 2.5 * field


def kernel_hamiltonian(extended, local_potential):
    interior = extended[:, 2:-2]
    along_first = (
        -1.0 / 12.0 * (extended[:, :-4] + extended[:, 4:])
        + 4.0 / 3.0 * (extended[:, 1:-3] + extended[:, 3:-1])
        - 2.5 * interior
    )
    laplace = along_first + kernel_lap(interior, 2) + kernel_lap(interior, 3)
    return -0.5 * laplace + local_potential[None] * interior


def kernel_shifted(extended, local_potential):
    return (kernel_hamiltonian(extended, local_potential) - center * extended[:, 2:-2]) / halfwidth


def filter_kernel(*refs):
    *piece_refs, pot_ref, filtered_ref, applied_ref = refs
    wide = jnp.concatenate([r[...] for r in piece_refs], axis=1)
    pot = pot_ref[...]
    first_term = kernel_shifted(wide, pot)
    filtered_wide = 2.0 * kernel_shifted(first_term, pot[2:-2]) - wide[:, 4:-4]
    filtered_ref[...] = filtered_wide[:, 2:-2]
    applied_ref[...] = kernel_hamiltonian(filtered_wide, pot[4:-4])


def filter_and_apply(pieces, pot_wide, group=8):
    bands, n = pieces[len(pieces) // 2].shape[:2]
    tail = pieces[0].shape[2:]

    def spec(planes):
        return pl.BlockSpec((group, planes) + tail, lambda i: (i, 0, 0, 0))

    out = jax.ShapeDtypeStruct((bands, n) + tail, jnp.float32)
    return pl.pallas_call(
        filter_kernel,
        grid=(bands // group,),
        in_specs=[spec(p.shape[1]) for p in pieces]
        + [pl.BlockSpec(pot_wide.shape, lambda i: (0, 0, 0))],
        out_specs=[spec(n), spec(n)],
        out_shape=[out, out],
        compiler_params=pltpu.CompilerParams(vmem_limit_bytes=48 * 1024 * 1024),
    )(*pieces, pot_wide)


def body(psi, potential, owner):
    pot_wide = jnp.concatenate(face_pieces(potential, 0, "dom", 4), axis=0)
    current, applied = filter_and_apply(face_pieces(psi, 1, "dom", 6), pot_wide)
    local_bands = current.shape[0]
    owner_root = owner[0]
    owned_panel = broadcast(current, "band", owner_root)
    total_cells = current.shape[1] * current.shape[2] * current.shape[3] * lax.axis_size("dom")
    scale = 1.0 / total_cells
    flattened = current.reshape(local_bands, -1)
    panel_flat = owned_panel.reshape(local_bands, -1)
    ham_rows = jnp.einsum(
        "pc,bc->pb", panel_flat, applied.reshape(local_bands, -1), precision=lax.Precision.HIGHEST
    )
    over_rows = jnp.einsum("pc,bc->pb", panel_flat, flattened, precision=lax.Precision.HIGHEST)
    both = doubling_sum(jnp.stack([over_rows * scale, ham_rows * scale]), "dom")
    return (current, both[0], both[1])


def solution(mesh):
    placed = (P("band", "dom", None, None), P("dom", None, None), P())
    return jax.shard_map(
        body,
        mesh=mesh,
        in_specs=placed,
        out_specs=(P("band", "dom", None, None), P(None, "band"), P(None, "band")),
        check_vma=False,
    )
```

```python
import jax
import jax.numpy as jnp
from jax import lax
from jax.experimental import pallas as pl
from jax.experimental.pallas import tpu as pltpu
from jax.sharding import PartitionSpec as P


center = 4.9
halfwidth = 4.1


def broadcast(array, axis, root):
    count = lax.axis_size(axis)
    piece = array.shape[0] // count
    spread = lax.all_to_all(array, axis, 0, 0, tiled=True)
    mine = lax.dynamic_slice_in_dim(spread, root * piece, piece, 0)
    repeated = jnp.broadcast_to(mine[None], (count,) + mine.shape).reshape(array.shape)
    return lax.all_to_all(repeated, axis, 0, 0, tiled=True)


def doubling_sum(array, axis):
    count = lax.axis_size(axis)
    step = 1
    while step < count:
        array = array + lax.ppermute(array, axis, [(i, i ^ step) for i in range(count)])
        step *= 2
    return array


def lap_periodic(grid_field, which_axis):
    outer = jnp.roll(grid_field, 2, which_axis) + jnp.roll(grid_field, -2, which_axis)
    nearer = jnp.roll(grid_field, 1, which_axis) + jnp.roll(grid_field, -1, which_axis)
    return -1.0 / 12.0 * outer + 4.0 / 3.0 * nearer - 2.5 * grid_field


def hamiltonian_apply(extended, local_potential):
    interior = extended[:, 2:-2]
    along_first = (
        -1.0 / 12.0 * (extended[:, :-4] + extended[:, 4:])
        + 4.0 / 3.0 * (extended[:, 1:-3] + extended[:, 3:-1])
        - 2.5 * interior
    )
    laplace = along_first + lap_periodic(interior, 2) + lap_periodic(interior, 3)
    return -0.5 * laplace + local_potential * interior


def shifted(extended, local_potential):
    return (hamiltonian_apply(extended, local_potential) - center * extended[:, 2:-2]) / halfwidth


def shifted_to(block, axis, shift):
    count = lax.axis_size(axis)
    return lax.ppermute(block, axis, [(i, (i + shift) % count) for i in range(count)])


def face_pieces(block, dim, axis, width):
    n = block.shape[dim]
    low, high = [], []
    for hop in range(1, -(-width // n) + 1):
        take = min(n, width - n * (hop - 1))
        low.insert(0, shifted_to(lax.slice_in_dim(block, n - take, None, axis=dim), axis, hop))
        high.append(shifted_to(lax.slice_in_dim(block, 0, take, axis=dim), axis, -hop))
    return low + [block] + high


def kernel_lap(field, which_axis):
    size = field.shape[which_axis]
    outer = pltpu.roll(field, 2, which_axis) + pltpu.roll(field, size - 2, which_axis)
    nearer = pltpu.roll(field, 1, which_axis) + pltpu.roll(field, size - 1, which_axis)
    return -1.0 / 12.0 * outer + 4.0 / 3.0 * nearer - 2.5 * field


def kernel_hamiltonian(extended, local_potential):
    interior = extended[:, 2:-2]
    along_first = (
        -1.0 / 12.0 * (extended[:, :-4] + extended[:, 4:])
        + 4.0 / 3.0 * (extended[:, 1:-3] + extended[:, 3:-1])
        - 2.5 * interior
    )
    laplace = along_first + kernel_lap(interior, 2) + kernel_lap(interior, 3)
    return -0.5 * laplace + local_potential[None] * interior


def kernel_shifted(extended, local_potential):
    return (kernel_hamiltonian(extended, local_potential) - center * extended[:, 2:-2]) / halfwidth


def filter_kernel(*refs):
    *piece_refs, pot_ref, filtered_ref, applied_ref = refs
    wide = jnp.concatenate([r[...] for r in piece_refs], axis=1)
    pot = pot_ref[...]
    first_term = kernel_shifted(wide, pot)
    filtered_wide = 2.0 * kernel_shifted(first_term, pot[2:-2]) - wide[:, 4:-4]
    filtered_ref[...] = filtered_wide[:, 2:-2]
    applied_ref[...] = kernel_hamiltonian(filtered_wide, pot[4:-4])


def filter_and_apply(pieces, pot_wide, group=8):
    bands, n = pieces[len(pieces) // 2].shape[:2]
    tail = pieces[0].shape[2:]

    def spec(planes):
        return pl.BlockSpec((group, planes) + tail, lambda i: (i, 0, 0, 0))

    out = jax.ShapeDtypeStruct((bands, n) + tail, jnp.float32)
    return pl.pallas_call(
        filter_kernel,
        grid=(bands // group,),
        in_specs=[spec(p.shape[1]) for p in pieces]
        + [pl.BlockSpec(pot_wide.shape, lambda i: (0, 0, 0))],
        out_specs=[spec(n), spec(n)],
        out_shape=[out, out],
        compiler_params=pltpu.CompilerParams(vmem_limit_bytes=48 * 1024 * 1024),
    )(*pieces, pot_wide)


def body(psi, potential, owner, stages=2):
    pot_wide = jnp.concatenate(face_pieces(potential, 0, "dom", 4), axis=0)
    owner_root = owner[0]
    step = psi.shape[0] // stages
    parts = []
    for stage in range(stages):
        block = lax.slice_in_dim(psi, stage * step, (stage + 1) * step, axis=0)
        filtered, applied = filter_and_apply(face_pieces(block, 1, "dom", 6), pot_wide)
        parts.append((filtered, applied, broadcast(filtered, "band", owner_root)))
    current, applied, owned_panel = (jnp.concatenate(p, axis=0) for p in zip(*parts))
    local_bands = current.shape[0]
    total_cells = current.shape[1] * current.shape[2] * current.shape[3] * lax.axis_size("dom")
    scale = 1.0 / total_cells
    flattened = current.reshape(local_bands, -1)
    panel_flat = owned_panel.reshape(local_bands, -1)
    ham_rows = jnp.einsum(
        "pc,bc->pb", panel_flat, applied.reshape(local_bands, -1), precision=lax.Precision.HIGHEST
    )
    over_rows = jnp.einsum("pc,bc->pb", panel_flat, flattened, precision=lax.Precision.HIGHEST)
    both = doubling_sum(jnp.stack([over_rows * scale, ham_rows * scale]), "dom")
    return (current, both[0], both[1])


def solution(mesh):
    placed = (P("band", "dom", None, None), P("dom", None, None), P())
    return jax.shard_map(
        body,
        mesh=mesh,
        in_specs=placed,
        out_specs=(P("band", "dom", None, None), P(None, "band"), P(None, "band")),
        check_vma=False,
    )
```

```python
import jax
import jax.numpy as jnp
from jax import lax
from jax.experimental import pallas as pl
from jax.experimental.pallas import tpu as pltpu
from jax.sharding import PartitionSpec as P


center = 4.9
halfwidth = 4.1


def broadcast(array, axis, root):
    count = lax.axis_size(axis)
    piece = array.shape[0] // count
    spread = lax.all_to_all(array, axis, 0, 0, tiled=True)
    mine = lax.dynamic_slice_in_dim(spread, root * piece, piece, 0)
    repeated = jnp.broadcast_to(mine[None], (count,) + mine.shape).reshape(array.shape)
    return lax.all_to_all(repeated, axis, 0, 0, tiled=True)


def doubling_sum(array, axis):
    count = lax.axis_size(axis)
    step = 1
    while step < count:
        array = array + lax.ppermute(array, axis, [(i, i ^ step) for i in range(count)])
        step *= 2
    return array


def lap_periodic(grid_field, which_axis):
    outer = jnp.roll(grid_field, 2, which_axis) + jnp.roll(grid_field, -2, which_axis)
    nearer = jnp.roll(grid_field, 1, which_axis) + jnp.roll(grid_field, -1, which_axis)
    return -1.0 / 12.0 * outer + 4.0 / 3.0 * nearer - 2.5 * grid_field


def hamiltonian_apply(extended, local_potential):
    interior = extended[:, 2:-2]
    along_first = (
        -1.0 / 12.0 * (extended[:, :-4] + extended[:, 4:])
        + 4.0 / 3.0 * (extended[:, 1:-3] + extended[:, 3:-1])
        - 2.5 * interior
    )
    laplace = along_first + lap_periodic(interior, 2) + lap_periodic(interior, 3)
    return -0.5 * laplace + local_potential * interior


def shifted(extended, local_potential):
    return (hamiltonian_apply(extended, local_potential) - center * extended[:, 2:-2]) / halfwidth


def shifted_to(block, axis, shift):
    count = lax.axis_size(axis)
    return lax.ppermute(block, axis, [(i, (i + shift) % count) for i in range(count)])


def face_pieces(block, dim, axis, width):
    n = block.shape[dim]
    low, high = [], []
    for hop in range(1, -(-width // n) + 1):
        take = min(n, width - n * (hop - 1))
        low.insert(0, shifted_to(lax.slice_in_dim(block, n - take, None, axis=dim), axis, hop))
        high.append(shifted_to(lax.slice_in_dim(block, 0, take, axis=dim), axis, -hop))
    return low + [block] + high


def kernel_lap(field, which_axis):
    size = field.shape[which_axis]
    outer = pltpu.roll(field, 2, which_axis) + pltpu.roll(field, size - 2, which_axis)
    nearer = pltpu.roll(field, 1, which_axis) + pltpu.roll(field, size - 1, which_axis)
    return -1.0 / 12.0 * outer + 4.0 / 3.0 * nearer - 2.5 * field


def kernel_hamiltonian(extended, local_potential):
    interior = extended[:, 2:-2]
    along_first = (
        -1.0 / 12.0 * (extended[:, :-4] + extended[:, 4:])
        + 4.0 / 3.0 * (extended[:, 1:-3] + extended[:, 3:-1])
        - 2.5 * interior
    )
    laplace = along_first + kernel_lap(interior, 2) + kernel_lap(interior, 3)
    return -0.5 * laplace + local_potential[None] * interior


def kernel_shifted(extended, local_potential):
    return (kernel_hamiltonian(extended, local_potential) - center * extended[:, 2:-2]) / halfwidth


def filter_kernel(*refs):
    *piece_refs, pot_ref, filtered_ref, applied_ref = refs
    wide = jnp.concatenate([r[...] for r in piece_refs], axis=1)
    pot = pot_ref[...]
    first_term = kernel_shifted(wide, pot)
    filtered_wide = 2.0 * kernel_shifted(first_term, pot[2:-2]) - wide[:, 4:-4]
    filtered_ref[...] = filtered_wide[:, 2:-2]
    applied_ref[...] = kernel_hamiltonian(filtered_wide, pot[4:-4])


def filter_and_apply(pieces, pot_wide, group=8):
    bands, n = pieces[len(pieces) // 2].shape[:2]
    tail = pieces[0].shape[2:]

    def spec(planes):
        return pl.BlockSpec((group, planes) + tail, lambda i: (i, 0, 0, 0))

    out = jax.ShapeDtypeStruct((bands, n) + tail, jnp.float32)
    return pl.pallas_call(
        filter_kernel,
        grid=(bands // group,),
        in_specs=[spec(p.shape[1]) for p in pieces]
        + [pl.BlockSpec(pot_wide.shape, lambda i: (0, 0, 0))],
        out_specs=[spec(n), spec(n)],
        out_shape=[out, out],
        compiler_params=pltpu.CompilerParams(vmem_limit_bytes=48 * 1024 * 1024),
    )(*pieces, pot_wide)


def body(psi, potential, owner, stages=1):
    pot_wide = jnp.concatenate(face_pieces(potential, 0, "dom", 4), axis=0)
    owner_root = owner[0]
    step = psi.shape[0] // stages
    parts = []
    for stage in range(stages):
        block = lax.slice_in_dim(psi, stage * step, (stage + 1) * step, axis=0)
        filtered, applied = filter_and_apply(face_pieces(block, 1, "dom", 6), pot_wide)
        parts.append((filtered, applied, broadcast(filtered, "band", owner_root)))
    current, applied, owned_panel = (jnp.concatenate(p, axis=0) for p in zip(*parts))
    local_bands = current.shape[0]
    total_cells = current.shape[1] * current.shape[2] * current.shape[3] * lax.axis_size("dom")
    scale = 1.0 / total_cells
    flattened = current.reshape(local_bands, -1)
    panel_flat = owned_panel.reshape(local_bands, -1)
    ham_rows = jnp.einsum(
        "pc,bc->pb", panel_flat, applied.reshape(local_bands, -1), precision=lax.Precision.HIGHEST
    )
    over_rows = jnp.einsum("pc,bc->pb", panel_flat, flattened, precision=lax.Precision.HIGHEST)
    both = doubling_sum(jnp.stack([over_rows * scale, ham_rows * scale]), "dom")
    return (current, both[0], both[1])


def solution(mesh):
    placed = (P("band", "dom", None, None), P("dom", None, None), P())
    return jax.shard_map(
        body,
        mesh=mesh,
        in_specs=placed,
        out_specs=(P("band", "dom", None, None), P(None, "band"), P(None, "band")),
        check_vma=False,
    )
```

```python
import jax
import jax.numpy as jnp
from jax import lax
from jax.experimental import pallas as pl
from jax.experimental.pallas import tpu as pltpu
from jax.sharding import PartitionSpec as P


center = 4.9
halfwidth = 4.1


def broadcast(array, axis, root):
    count = lax.axis_size(axis)
    piece = array.shape[0] // count
    spread = lax.all_to_all(array, axis, 0, 0, tiled=True)
    mine = lax.dynamic_slice_in_dim(spread, root * piece, piece, 0)
    repeated = jnp.broadcast_to(mine[None], (count,) + mine.shape).reshape(array.shape)
    return lax.all_to_all(repeated, axis, 0, 0, tiled=True)


def doubling_sum(array, axis):
    count = lax.axis_size(axis)
    step = 1
    while step < count:
        array = array + lax.ppermute(array, axis, [(i, i ^ step) for i in range(count)])
        step *= 2
    return array


def lap_periodic(grid_field, which_axis):
    outer = jnp.roll(grid_field, 2, which_axis) + jnp.roll(grid_field, -2, which_axis)
    nearer = jnp.roll(grid_field, 1, which_axis) + jnp.roll(grid_field, -1, which_axis)
    return -1.0 / 12.0 * outer + 4.0 / 3.0 * nearer - 2.5 * grid_field


def hamiltonian_apply(extended, local_potential):
    interior = extended[:, 2:-2]
    along_first = (
        -1.0 / 12.0 * (extended[:, :-4] + extended[:, 4:])
        + 4.0 / 3.0 * (extended[:, 1:-3] + extended[:, 3:-1])
        - 2.5 * interior
    )
    laplace = along_first + lap_periodic(interior, 2) + lap_periodic(interior, 3)
    return -0.5 * laplace + local_potential * interior


def shifted(extended, local_potential):
    return (hamiltonian_apply(extended, local_potential) - center * extended[:, 2:-2]) / halfwidth


def shifted_to(block, axis, shift):
    count = lax.axis_size(axis)
    return lax.ppermute(block, axis, [(i, (i + shift) % count) for i in range(count)])


def face_pieces(block, dim, axis, width):
    n = block.shape[dim]
    low, high = [], []
    for hop in range(1, -(-width // n) + 1):
        take = min(n, width - n * (hop - 1))
        low.insert(0, shifted_to(lax.slice_in_dim(block, n - take, None, axis=dim), axis, hop))
        high.append(shifted_to(lax.slice_in_dim(block, 0, take, axis=dim), axis, -hop))
    return low + [block] + high


def kernel_lap(field, which_axis):
    size = field.shape[which_axis]
    outer = pltpu.roll(field, 2, which_axis) + pltpu.roll(field, size - 2, which_axis)
    nearer = pltpu.roll(field, 1, which_axis) + pltpu.roll(field, size - 1, which_axis)
    return -1.0 / 12.0 * outer + 4.0 / 3.0 * nearer - 2.5 * field


def kernel_hamiltonian(extended, local_potential):
    interior = extended[:, 2:-2]
    along_first = (
        -1.0 / 12.0 * (extended[:, :-4] + extended[:, 4:])
        + 4.0 / 3.0 * (extended[:, 1:-3] + extended[:, 3:-1])
        - 2.5 * interior
    )
    laplace = along_first + kernel_lap(interior, 2) + kernel_lap(interior, 3)
    return -0.5 * laplace + local_potential[None] * interior


def kernel_shifted(extended, local_potential):
    return (kernel_hamiltonian(extended, local_potential) - center * extended[:, 2:-2]) / halfwidth


def filter_kernel(*refs):
    *piece_refs, pot_ref, filtered_ref, applied_ref = refs
    wide = jnp.concatenate([r[...] for r in piece_refs], axis=1)
    pot = pot_ref[...]
    first_term = kernel_shifted(wide, pot)
    filtered_wide = 2.0 * kernel_shifted(first_term, pot[2:-2]) - wide[:, 4:-4]
    filtered_ref[...] = filtered_wide[:, 2:-2]
    applied_ref[...] = kernel_hamiltonian(filtered_wide, pot[4:-4])


def filter_and_apply(pieces, pot_wide, group=8):
    bands, n = pieces[len(pieces) // 2].shape[:2]
    tail = pieces[0].shape[2:]

    def spec(planes):
        return pl.BlockSpec((group, planes) + tail, lambda i: (i, 0, 0, 0))

    out = jax.ShapeDtypeStruct((bands, n) + tail, jnp.float32)
    return pl.pallas_call(
        filter_kernel,
        grid=(bands // group,),
        in_specs=[spec(p.shape[1]) for p in pieces]
        + [pl.BlockSpec(pot_wide.shape, lambda i: (0, 0, 0))],
        out_specs=[spec(n), spec(n)],
        out_shape=[out, out],
        compiler_params=pltpu.CompilerParams(vmem_limit_bytes=48 * 1024 * 1024),
    )(*pieces, pot_wide)


def body(psi, potential, owner):
    bands, n = psi.shape[:2]
    if n >= 4:
        pieces = face_pieces(jnp.concatenate([psi, potential[None]], axis=0), 1, "dom", 6)
        mid = len(pieces) // 2
        low, high = pieces[mid - 1][bands], pieces[mid + 1][bands]
        pot_wide = jnp.concatenate([low[-4:], potential, high[:4]], axis=0)
        pieces = [p[:bands] for p in pieces]
    else:
        pot_wide = jnp.concatenate(face_pieces(potential, 0, "dom", 4), axis=0)
        pieces = face_pieces(psi, 1, "dom", 6)
    current, applied = filter_and_apply(pieces, pot_wide)
    owner_root = owner[0]
    owned_panel = broadcast(current, "band", owner_root)
    local_bands = current.shape[0]
    total_cells = current.shape[1] * current.shape[2] * current.shape[3] * lax.axis_size("dom")
    scale = 1.0 / total_cells
    flattened = current.reshape(local_bands, -1)
    panel_flat = owned_panel.reshape(local_bands, -1)
    ham_rows = jnp.einsum(
        "pc,bc->pb", panel_flat, applied.reshape(local_bands, -1), precision=lax.Precision.HIGHEST
    )
    over_rows = jnp.einsum("pc,bc->pb", panel_flat, flattened, precision=lax.Precision.HIGHEST)
    both = doubling_sum(jnp.stack([over_rows * scale, ham_rows * scale]), "dom")
    return (current, both[0], both[1])


def solution(mesh):
    placed = (P("band", "dom", None, None), P("dom", None, None), P())
    return jax.shard_map(
        body,
        mesh=mesh,
        in_specs=placed,
        out_specs=(P("band", "dom", None, None), P(None, "band"), P(None, "band")),
        check_vma=False,
    )
```

```python
import jax
import jax.numpy as jnp
from jax import lax
from jax.experimental import pallas as pl
from jax.experimental.pallas import tpu as pltpu
from jax.sharding import PartitionSpec as P


center = 4.9
halfwidth = 4.1


def broadcast(array, axis, root):
    count = lax.axis_size(axis)
    piece = array.shape[0] // count
    spread = lax.all_to_all(array, axis, 0, 0, tiled=True)
    mine = lax.dynamic_slice_in_dim(spread, root * piece, piece, 0)
    repeated = jnp.broadcast_to(mine[None], (count,) + mine.shape).reshape(array.shape)
    return lax.all_to_all(repeated, axis, 0, 0, tiled=True)


def doubling_sum(array, axis):
    count = lax.axis_size(axis)
    step = 1
    while step < count:
        array = array + lax.ppermute(array, axis, [(i, i ^ step) for i in range(count)])
        step *= 2
    return array


def lap_periodic(grid_field, which_axis):
    outer = jnp.roll(grid_field, 2, which_axis) + jnp.roll(grid_field, -2, which_axis)
    nearer = jnp.roll(grid_field, 1, which_axis) + jnp.roll(grid_field, -1, which_axis)
    return -1.0 / 12.0 * outer + 4.0 / 3.0 * nearer - 2.5 * grid_field


def hamiltonian_apply(extended, local_potential):
    interior = extended[:, 2:-2]
    along_first = (
        -1.0 / 12.0 * (extended[:, :-4] + extended[:, 4:])
        + 4.0 / 3.0 * (extended[:, 1:-3] + extended[:, 3:-1])
        - 2.5 * interior
    )
    laplace = along_first + lap_periodic(interior, 2) + lap_periodic(interior, 3)
    return -0.5 * laplace + local_potential * interior


def shifted(extended, local_potential):
    return (hamiltonian_apply(extended, local_potential) - center * extended[:, 2:-2]) / halfwidth


def shifted_to(block, axis, shift):
    count = lax.axis_size(axis)
    return lax.ppermute(block, axis, [(i, (i + shift) % count) for i in range(count)])


def face_pieces(block, dim, axis, width):
    n = block.shape[dim]
    low, high = [], []
    for hop in range(1, -(-width // n) + 1):
        take = min(n, width - n * (hop - 1))
        low.insert(0, shifted_to(lax.slice_in_dim(block, n - take, None, axis=dim), axis, hop))
        high.append(shifted_to(lax.slice_in_dim(block, 0, take, axis=dim), axis, -hop))
    return low + [block] + high


def kernel_lap(field, which_axis):
    size = field.shape[which_axis]
    outer = pltpu.roll(field, 2, which_axis) + pltpu.roll(field, size - 2, which_axis)
    nearer = pltpu.roll(field, 1, which_axis) + pltpu.roll(field, size - 1, which_axis)
    return -1.0 / 12.0 * outer + 4.0 / 3.0 * nearer - 2.5 * field


def kernel_hamiltonian(extended, local_potential):
    interior = extended[:, 2:-2]
    along_first = (
        -1.0 / 12.0 * (extended[:, :-4] + extended[:, 4:])
        + 4.0 / 3.0 * (extended[:, 1:-3] + extended[:, 3:-1])
        - 2.5 * interior
    )
    laplace = along_first + kernel_lap(interior, 2) + kernel_lap(interior, 3)
    return -0.5 * laplace + local_potential[None] * interior


def kernel_shifted(extended, local_potential):
    return (kernel_hamiltonian(extended, local_potential) - center * extended[:, 2:-2]) * (1.0 / halfwidth)


def filter_kernel(*refs):
    *piece_refs, pot_ref, filtered_ref, applied_ref = refs
    wide = jnp.concatenate([r[...] for r in piece_refs], axis=1)
    pot = pot_ref[...]
    first_term = kernel_shifted(wide, pot)
    filtered_wide = 2.0 * kernel_shifted(first_term, pot[2:-2]) - wide[:, 4:-4]
    filtered_ref[...] = filtered_wide[:, 2:-2]
    applied_ref[...] = kernel_hamiltonian(filtered_wide, pot[4:-4])


def filter_and_apply(pieces, pot_wide, group=8):
    bands, n = pieces[len(pieces) // 2].shape[:2]
    tail = pieces[0].shape[2:]

    def spec(planes):
        return pl.BlockSpec((group, planes) + tail, lambda i: (i, 0, 0, 0))

    out = jax.ShapeDtypeStruct((bands, n) + tail, jnp.float32)
    return pl.pallas_call(
        filter_kernel,
        grid=(bands // group,),
        in_specs=[spec(p.shape[1]) for p in pieces]
        + [pl.BlockSpec(pot_wide.shape, lambda i: (0, 0, 0))],
        out_specs=[spec(n), spec(n)],
        out_shape=[out, out],
        compiler_params=pltpu.CompilerParams(vmem_limit_bytes=48 * 1024 * 1024),
    )(*pieces, pot_wide)


def body(psi, potential, owner, stages=1):
    pot_wide = jnp.concatenate(face_pieces(potential, 0, "dom", 4), axis=0)
    owner_root = owner[0]
    step = psi.shape[0] // stages
    parts = []
    for stage in range(stages):
        block = lax.slice_in_dim(psi, stage * step, (stage + 1) * step, axis=0)
        filtered, applied = filter_and_apply(face_pieces(block, 1, "dom", 6), pot_wide)
        parts.append((filtered, applied, broadcast(filtered, "band", owner_root)))
    current, applied, owned_panel = (jnp.concatenate(p, axis=0) for p in zip(*parts))
    local_bands = current.shape[0]
    total_cells = current.shape[1] * current.shape[2] * current.shape[3] * lax.axis_size("dom")
    scale = 1.0 / total_cells
    flattened = current.reshape(local_bands, -1)
    panel_flat = owned_panel.reshape(local_bands, -1)
    ham_rows = jnp.einsum(
        "pc,bc->pb", panel_flat, applied.reshape(local_bands, -1), precision=lax.Precision.HIGHEST
    )
    over_rows = jnp.einsum("pc,bc->pb", panel_flat, flattened, precision=lax.Precision.HIGHEST)
    both = doubling_sum(jnp.stack([over_rows * scale, ham_rows * scale]), "dom")
    return (current, both[0], both[1])


def solution(mesh):
    placed = (P("band", "dom", None, None), P("dom", None, None), P())
    return jax.shard_map(
        body,
        mesh=mesh,
        in_specs=placed,
        out_specs=(P("band", "dom", None, None), P(None, "band"), P(None, "band")),
        check_vma=False,
    )
```

```python
import jax
import jax.numpy as jnp
from jax import lax
from jax.experimental import pallas as pl
from jax.experimental.pallas import tpu as pltpu
from jax.sharding import PartitionSpec as P


center = 4.9
halfwidth = 4.1


def broadcast(array, axis, root):
    count = lax.axis_size(axis)
    piece = array.shape[0] // count
    spread = lax.all_to_all(array, axis, 0, 0, tiled=True)
    mine = lax.dynamic_slice_in_dim(spread, root * piece, piece, 0)
    repeated = jnp.broadcast_to(mine[None], (count,) + mine.shape).reshape(array.shape)
    return lax.all_to_all(repeated, axis, 0, 0, tiled=True)


def doubling_sum(array, axis):
    count = lax.axis_size(axis)
    step = 1
    while step < count:
        array = array + lax.ppermute(array, axis, [(i, i ^ step) for i in range(count)])
        step *= 2
    return array


def lap_periodic(grid_field, which_axis):
    outer = jnp.roll(grid_field, 2, which_axis) + jnp.roll(grid_field, -2, which_axis)
    nearer = jnp.roll(grid_field, 1, which_axis) + jnp.roll(grid_field, -1, which_axis)
    return -1.0 / 12.0 * outer + 4.0 / 3.0 * nearer - 2.5 * grid_field


def hamiltonian_apply(extended, local_potential):
    interior = extended[:, 2:-2]
    along_first = (
        -1.0 / 12.0 * (extended[:, :-4] + extended[:, 4:])
        + 4.0 / 3.0 * (extended[:, 1:-3] + extended[:, 3:-1])
        - 2.5 * interior
    )
    laplace = along_first + lap_periodic(interior, 2) + lap_periodic(interior, 3)
    return -0.5 * laplace + local_potential * interior


def shifted(extended, local_potential):
    return (hamiltonian_apply(extended, local_potential) - center * extended[:, 2:-2]) / halfwidth


def shifted_to(block, axis, shift):
    count = lax.axis_size(axis)
    return lax.ppermute(block, axis, [(i, (i + shift) % count) for i in range(count)])


def face_pieces(block, dim, axis, width):
    n = block.shape[dim]
    low, high = [], []
    for hop in range(1, -(-width // n) + 1):
        take = min(n, width - n * (hop - 1))
        low.insert(0, shifted_to(lax.slice_in_dim(block, n - take, None, axis=dim), axis, hop))
        high.append(shifted_to(lax.slice_in_dim(block, 0, take, axis=dim), axis, -hop))
    return low + [block] + high


def kernel_lap(field, which_axis):
    size = field.shape[which_axis]
    outer = pltpu.roll(field, 2, which_axis) + pltpu.roll(field, size - 2, which_axis)
    nearer = pltpu.roll(field, 1, which_axis) + pltpu.roll(field, size - 1, which_axis)
    return -1.0 / 12.0 * outer + 4.0 / 3.0 * nearer - 2.5 * field


def kernel_hamiltonian(extended, local_potential):
    interior = extended[:, 2:-2]
    along_first = (
        -1.0 / 12.0 * (extended[:, :-4] + extended[:, 4:])
        + 4.0 / 3.0 * (extended[:, 1:-3] + extended[:, 3:-1])
        - 2.5 * interior
    )
    laplace = along_first + kernel_lap(interior, 2) + kernel_lap(interior, 3)
    return -0.5 * laplace + local_potential[None] * interior


def kernel_shifted(extended, local_potential):
    return (kernel_hamiltonian(extended, local_potential) - center * extended[:, 2:-2]) / halfwidth


def filter_kernel(*refs):
    *piece_refs, pot_ref, filtered_ref, applied_ref = refs
    pot = pot_ref[...]

    def one_band(band, carry):
        rows = pl.ds(band, 1)
        wide = jnp.concatenate([r[rows] for r in piece_refs], axis=1)
        first_term = kernel_shifted(wide, pot)
        filtered_wide = 2.0 * kernel_shifted(first_term, pot[2:-2]) - wide[:, 4:-4]
        filtered_ref[rows] = filtered_wide[:, 2:-2]
        applied_ref[rows] = kernel_hamiltonian(filtered_wide, pot[4:-4])
        return carry

    lax.fori_loop(0, filtered_ref.shape[0], one_band, 0)


def filter_and_apply(pieces, pot_wide, group=8):
    bands, n = pieces[len(pieces) // 2].shape[:2]
    tail = pieces[0].shape[2:]

    def spec(planes):
        return pl.BlockSpec((group, planes) + tail, lambda i: (i, 0, 0, 0))

    out = jax.ShapeDtypeStruct((bands, n) + tail, jnp.float32)
    return pl.pallas_call(
        filter_kernel,
        grid=(bands // group,),
        in_specs=[spec(p.shape[1]) for p in pieces]
        + [pl.BlockSpec(pot_wide.shape, lambda i: (0, 0, 0))],
        out_specs=[spec(n), spec(n)],
        out_shape=[out, out],
        compiler_params=pltpu.CompilerParams(vmem_limit_bytes=48 * 1024 * 1024),
    )(*pieces, pot_wide)


def body(psi, potential, owner, stages=1):
    pot_wide = jnp.concatenate(face_pieces(potential, 0, "dom", 4), axis=0)
    owner_root = owner[0]
    step = psi.shape[0] // stages
    parts = []
    for stage in range(stages):
        block = lax.slice_in_dim(psi, stage * step, (stage + 1) * step, axis=0)
        filtered, applied = filter_and_apply(face_pieces(block, 1, "dom", 6), pot_wide)
        parts.append((filtered, applied, broadcast(filtered, "band", owner_root)))
    current, applied, owned_panel = (jnp.concatenate(p, axis=0) for p in zip(*parts))
    local_bands = current.shape[0]
    total_cells = current.shape[1] * current.shape[2] * current.shape[3] * lax.axis_size("dom")
    scale = 1.0 / total_cells
    flattened = current.reshape(local_bands, -1)
    panel_flat = owned_panel.reshape(local_bands, -1)
    ham_rows = jnp.einsum(
        "pc,bc->pb", panel_flat, applied.reshape(local_bands, -1), precision=lax.Precision.HIGHEST
    )
    over_rows = jnp.einsum("pc,bc->pb", panel_flat, flattened, precision=lax.Precision.HIGHEST)
    both = doubling_sum(jnp.stack([over_rows * scale, ham_rows * scale]), "dom")
    return (current, both[0], both[1])


def solution(mesh):
    placed = (P("band", "dom", None, None), P("dom", None, None), P())
    return jax.shard_map(
        body,
        mesh=mesh,
        in_specs=placed,
        out_specs=(P("band", "dom", None, None), P(None, "band"), P(None, "band")),
        check_vma=False,
    )
```

```python
import jax
import jax.numpy as jnp
from jax import lax
from jax.experimental import pallas as pl
from jax.experimental.pallas import tpu as pltpu
from jax.sharding import PartitionSpec as P


center = 4.9
halfwidth = 4.1


def broadcast(array, axis, root):
    count = lax.axis_size(axis)
    piece = array.shape[0] // count
    spread = lax.all_to_all(array, axis, 0, 0, tiled=True)
    mine = lax.dynamic_slice_in_dim(spread, root * piece, piece, 0)
    repeated = jnp.broadcast_to(mine[None], (count,) + mine.shape).reshape(array.shape)
    return lax.all_to_all(repeated, axis, 0, 0, tiled=True)


def doubling_sum(array, axis):
    count = lax.axis_size(axis)
    step = 1
    while step < count:
        array = array + lax.ppermute(array, axis, [(i, i ^ step) for i in range(count)])
        step *= 2
    return array


def lap_periodic(grid_field, which_axis):
    outer = jnp.roll(grid_field, 2, which_axis) + jnp.roll(grid_field, -2, which_axis)
    nearer = jnp.roll(grid_field, 1, which_axis) + jnp.roll(grid_field, -1, which_axis)
    return -1.0 / 12.0 * outer + 4.0 / 3.0 * nearer - 2.5 * grid_field


def hamiltonian_apply(extended, local_potential):
    interior = extended[:, 2:-2]
    along_first = (
        -1.0 / 12.0 * (extended[:, :-4] + extended[:, 4:])
        + 4.0 / 3.0 * (extended[:, 1:-3] + extended[:, 3:-1])
        - 2.5 * interior
    )
    laplace = along_first + lap_periodic(interior, 2) + lap_periodic(interior, 3)
    return -0.5 * laplace + local_potential * interior


def shifted(extended, local_potential):
    return (hamiltonian_apply(extended, local_potential) - center * extended[:, 2:-2]) / halfwidth


def shifted_to(block, axis, shift):
    count = lax.axis_size(axis)
    return lax.ppermute(block, axis, [(i, (i + shift) % count) for i in range(count)])


def face_pieces(block, dim, axis, width):
    n = block.shape[dim]
    low, high = [], []
    for hop in range(1, -(-width // n) + 1):
        take = min(n, width - n * (hop - 1))
        low.insert(0, shifted_to(lax.slice_in_dim(block, n - take, None, axis=dim), axis, hop))
        high.append(shifted_to(lax.slice_in_dim(block, 0, take, axis=dim), axis, -hop))
    return low + [block] + high


def kernel_lap(field, which_axis):
    size = field.shape[which_axis]
    outer = pltpu.roll(field, 2, which_axis) + pltpu.roll(field, size - 2, which_axis)
    nearer = pltpu.roll(field, 1, which_axis) + pltpu.roll(field, size - 1, which_axis)
    return -1.0 / 12.0 * outer + 4.0 / 3.0 * nearer - 2.5 * field


def kernel_hamiltonian(extended, local_potential):
    interior = extended[:, 2:-2]
    along_first = (
        -1.0 / 12.0 * (extended[:, :-4] + extended[:, 4:])
        + 4.0 / 3.0 * (extended[:, 1:-3] + extended[:, 3:-1])
        - 2.5 * interior
    )
    laplace = along_first + kernel_lap(interior, 2) + kernel_lap(interior, 3)
    return -0.5 * laplace + local_potential[None] * interior


def kernel_shifted(extended, local_potential):
    return (kernel_hamiltonian(extended, local_potential) - center * extended[:, 2:-2]) / halfwidth


def filter_kernel(*refs):
    *piece_refs, pot_ref, filtered_ref, low_ref, high_ref = refs
    wide = jnp.concatenate([r[...] for r in piece_refs], axis=1)
    pot = pot_ref[...]
    first_term = kernel_shifted(wide, pot)
    filtered_wide = 2.0 * kernel_shifted(first_term, pot[2:-2]) - wide[:, 4:-4]
    filtered_ref[...] = filtered_wide[:, 2:-2]
    low_ref[...] = filtered_wide[:, :2]
    high_ref[...] = filtered_wide[:, -2:]


def apply_kernel(low_ref, filtered_ref, high_ref, pot_ref, applied_ref):
    wide = jnp.concatenate([low_ref[...], filtered_ref[...], high_ref[...]], axis=1)
    applied_ref[...] = kernel_hamiltonian(wide, pot_ref[...])


def block_spec(group, planes, tail):
    return pl.BlockSpec((group, planes) + tail, lambda i: (i, 0, 0, 0))


def filter_only(pieces, pot_wide, group=8):
    bands, n = pieces[len(pieces) // 2].shape[:2]
    tail = pieces[0].shape[2:]
    shapes = [jax.ShapeDtypeStruct((bands, planes) + tail, jnp.float32) for planes in (n, 2, 2)]
    return pl.pallas_call(
        filter_kernel,
        grid=(bands // group,),
        in_specs=[block_spec(group, p.shape[1], tail) for p in pieces]
        + [pl.BlockSpec(pot_wide.shape, lambda i: (0, 0, 0))],
        out_specs=[block_spec(group, planes, tail) for planes in (n, 2, 2)],
        out_shape=shapes,
        compiler_params=pltpu.CompilerParams(vmem_limit_bytes=48 * 1024 * 1024),
    )(*pieces, pot_wide)


def apply_only(low, filtered, high, potential, group=8):
    bands, n = filtered.shape[:2]
    tail = filtered.shape[2:]
    return pl.pallas_call(
        apply_kernel,
        grid=(bands // group,),
        in_specs=[block_spec(group, 2, tail), block_spec(group, n, tail), block_spec(group, 2, tail)]
        + [pl.BlockSpec(potential.shape, lambda i: (0, 0, 0))],
        out_specs=block_spec(group, n, tail),
        out_shape=jax.ShapeDtypeStruct(filtered.shape, jnp.float32),
        compiler_params=pltpu.CompilerParams(vmem_limit_bytes=48 * 1024 * 1024),
    )(low, filtered, high, potential)


def body(psi, potential, owner, stages=1):
    pot_wide = jnp.concatenate(face_pieces(potential, 0, "dom", 4), axis=0)
    owner_root = owner[0]
    step = psi.shape[0] // stages
    parts = []
    for stage in range(stages):
        block = lax.slice_in_dim(psi, stage * step, (stage + 1) * step, axis=0)
        filtered, low, high = filter_only(face_pieces(block, 1, "dom", 6), pot_wide)
        panel = broadcast(filtered, "band", owner_root)
        parts.append((filtered, apply_only(low, filtered, high, potential), panel))
    current, applied, owned_panel = (jnp.concatenate(p, axis=0) for p in zip(*parts))
    local_bands = current.shape[0]
    total_cells = current.shape[1] * current.shape[2] * current.shape[3] * lax.axis_size("dom")
    scale = 1.0 / total_cells
    flattened = current.reshape(local_bands, -1)
    panel_flat = owned_panel.reshape(local_bands, -1)
    ham_rows = jnp.einsum(
        "pc,bc->pb", panel_flat, applied.reshape(local_bands, -1), precision=lax.Precision.HIGHEST
    )
    over_rows = jnp.einsum("pc,bc->pb", panel_flat, flattened, precision=lax.Precision.HIGHEST)
    both = doubling_sum(jnp.stack([over_rows * scale, ham_rows * scale]), "dom")
    return (current, both[0], both[1])


def solution(mesh):
    placed = (P("band", "dom", None, None), P("dom", None, None), P())
    return jax.shard_map(
        body,
        mesh=mesh,
        in_specs=placed,
        out_specs=(P("band", "dom", None, None), P(None, "band"), P(None, "band")),
        check_vma=False,
    )
```

```python
import jax
import jax.numpy as jnp
from jax import lax
from jax.experimental import pallas as pl
from jax.experimental.pallas import tpu as pltpu
from jax.sharding import PartitionSpec as P


center = 4.9
halfwidth = 4.1


def broadcast(array, axis, root):
    count = lax.axis_size(axis)
    piece = array.shape[0] // count
    spread = lax.all_to_all(array, axis, 0, 0, tiled=True)
    mine = lax.dynamic_slice_in_dim(spread, root * piece, piece, 0)
    repeated = jnp.broadcast_to(mine[None], (count,) + mine.shape).reshape(array.shape)
    return lax.all_to_all(repeated, axis, 0, 0, tiled=True)


def doubling_sum(array, axis):
    count = lax.axis_size(axis)
    step = 1
    while step < count:
        array = array + lax.ppermute(array, axis, [(i, i ^ step) for i in range(count)])
        step *= 2
    return array


def lap_periodic(grid_field, which_axis):
    outer = jnp.roll(grid_field, 2, which_axis) + jnp.roll(grid_field, -2, which_axis)
    nearer = jnp.roll(grid_field, 1, which_axis) + jnp.roll(grid_field, -1, which_axis)
    return -1.0 / 12.0 * outer + 4.0 / 3.0 * nearer - 2.5 * grid_field


def hamiltonian_apply(extended, local_potential):
    interior = extended[:, 2:-2]
    along_first = (
        -1.0 / 12.0 * (extended[:, :-4] + extended[:, 4:])
        + 4.0 / 3.0 * (extended[:, 1:-3] + extended[:, 3:-1])
        - 2.5 * interior
    )
    laplace = along_first + lap_periodic(interior, 2) + lap_periodic(interior, 3)
    return -0.5 * laplace + local_potential * interior


def shifted(extended, local_potential):
    return (hamiltonian_apply(extended, local_potential) - center * extended[:, 2:-2]) / halfwidth


def shifted_to(block, axis, shift):
    count = lax.axis_size(axis)
    return lax.ppermute(block, axis, [(i, (i + shift) % count) for i in range(count)])


def face_pieces(block, dim, axis, width):
    n = block.shape[dim]
    low, high = [], []
    for hop in range(1, -(-width // n) + 1):
        take = min(n, width - n * (hop - 1))
        low.insert(0, shifted_to(lax.slice_in_dim(block, n - take, None, axis=dim), axis, hop))
        high.append(shifted_to(lax.slice_in_dim(block, 0, take, axis=dim), axis, -hop))
    return low + [block] + high


def kernel_lap(field, which_axis):
    size = field.shape[which_axis]
    outer = pltpu.roll(field, 2, which_axis) + pltpu.roll(field, size - 2, which_axis)
    nearer = pltpu.roll(field, 1, which_axis) + pltpu.roll(field, size - 1, which_axis)
    return -1.0 / 12.0 * outer + 4.0 / 3.0 * nearer - 2.5 * field


def kernel_hamiltonian(extended, local_potential):
    interior = extended[:, 2:-2]
    along_first = (
        -1.0 / 12.0 * (extended[:, :-4] + extended[:, 4:])
        + 4.0 / 3.0 * (extended[:, 1:-3] + extended[:, 3:-1])
        - 2.5 * interior
    )
    laplace = along_first + kernel_lap(interior, 2) + kernel_lap(interior, 3)
    return -0.5 * laplace + local_potential[None] * interior


def kernel_shifted(extended, local_potential):
    return (kernel_hamiltonian(extended, local_potential) - center * extended[:, 2:-2]) / halfwidth


def kernel_stencil(extended, per_plane, outer_weight, near_weight):
    interior = extended[:, 2:-2]
    ny, nz = interior.shape[2], interior.shape[3]
    outer = (
        (extended[:, :-4] + extended[:, 4:])
        + (pltpu.roll(interior, 2, 2) + pltpu.roll(interior, ny - 2, 2))
        + (pltpu.roll(interior, 2, 3) + pltpu.roll(interior, nz - 2, 3))
    )
    nearer = (
        (extended[:, 1:-3] + extended[:, 3:-1])
        + (pltpu.roll(interior, 1, 2) + pltpu.roll(interior, ny - 1, 2))
        + (pltpu.roll(interior, 1, 3) + pltpu.roll(interior, nz - 1, 3))
    )
    return outer_weight * outer + near_weight * nearer + per_plane[None] * interior


def filter_kernel(*refs):
    *piece_refs, pot_ref, filtered_ref, applied_ref = refs
    wide = jnp.concatenate([r[...] for r in piece_refs], axis=1)
    pot = pot_ref[...]
    outer_h, near_h = 0.5 / 12.0, -0.5 * 4.0 / 3.0
    diagonal_h = pot + 7.5 * 0.5
    diagonal_s = (diagonal_h - center) / halfwidth
    first_term = kernel_stencil(wide, diagonal_s, outer_h / halfwidth, near_h / halfwidth)
    filtered_wide = (
        kernel_stencil(first_term, 2.0 * diagonal_s[2:-2], 2.0 * outer_h / halfwidth, 2.0 * near_h / halfwidth)
        - wide[:, 4:-4]
    )
    filtered_ref[...] = filtered_wide[:, 2:-2]
    applied_ref[...] = kernel_stencil(filtered_wide, diagonal_h[4:-4], outer_h, near_h)


def filter_and_apply(pieces, pot_wide, group=8):
    bands, n = pieces[len(pieces) // 2].shape[:2]
    tail = pieces[0].shape[2:]

    def spec(planes):
        return pl.BlockSpec((group, planes) + tail, lambda i: (i, 0, 0, 0))

    out = jax.ShapeDtypeStruct((bands, n) + tail, jnp.float32)
    return pl.pallas_call(
        filter_kernel,
        grid=(bands // group,),
        in_specs=[spec(p.shape[1]) for p in pieces]
        + [pl.BlockSpec(pot_wide.shape, lambda i: (0, 0, 0))],
        out_specs=[spec(n), spec(n)],
        out_shape=[out, out],
        compiler_params=pltpu.CompilerParams(vmem_limit_bytes=48 * 1024 * 1024),
    )(*pieces, pot_wide)


def body(psi, potential, owner, stages=1):
    pot_wide = jnp.concatenate(face_pieces(potential, 0, "dom", 4), axis=0)
    owner_root = owner[0]
    step = psi.shape[0] // stages
    parts = []
    for stage in range(stages):
        block = lax.slice_in_dim(psi, stage * step, (stage + 1) * step, axis=0)
        filtered, applied = filter_and_apply(face_pieces(block, 1, "dom", 6), pot_wide)
        parts.append((filtered, applied, broadcast(filtered, "band", owner_root)))
    current, applied, owned_panel = (jnp.concatenate(p, axis=0) for p in zip(*parts))
    local_bands = current.shape[0]
    total_cells = current.shape[1] * current.shape[2] * current.shape[3] * lax.axis_size("dom")
    scale = 1.0 / total_cells
    flattened = current.reshape(local_bands, -1)
    panel_flat = owned_panel.reshape(local_bands, -1)
    ham_rows = jnp.einsum(
        "pc,bc->pb", panel_flat, applied.reshape(local_bands, -1), precision=lax.Precision.HIGHEST
    )
    over_rows = jnp.einsum("pc,bc->pb", panel_flat, flattened, precision=lax.Precision.HIGHEST)
    both = doubling_sum(jnp.stack([over_rows * scale, ham_rows * scale]), "dom")
    return (current, both[0], both[1])


def solution(mesh):
    placed = (P("band", "dom", None, None), P("dom", None, None), P())
    return jax.shard_map(
        body,
        mesh=mesh,
        in_specs=placed,
        out_specs=(P("band", "dom", None, None), P(None, "band"), P(None, "band")),
        check_vma=False,
    )
```

```python
import jax
import jax.numpy as jnp
from jax import lax
from jax.experimental import pallas as pl
from jax.experimental.pallas import tpu as pltpu
from jax.sharding import PartitionSpec as P


center = 4.9
halfwidth = 4.1


def broadcast(array, axis, root):
    count = lax.axis_size(axis)
    piece = array.shape[0] // count
    spread = lax.all_to_all(array, axis, 0, 0, tiled=True)
    mine = lax.dynamic_slice_in_dim(spread, root * piece, piece, 0)
    repeated = jnp.broadcast_to(mine[None], (count,) + mine.shape).reshape(array.shape)
    return lax.all_to_all(repeated, axis, 0, 0, tiled=True)


def doubling_sum(array, axis):
    count = lax.axis_size(axis)
    step = 1
    while step < count:
        array = array + lax.ppermute(array, axis, [(i, i ^ step) for i in range(count)])
        step *= 2
    return array


def lap_periodic(grid_field, which_axis):
    outer = jnp.roll(grid_field, 2, which_axis) + jnp.roll(grid_field, -2, which_axis)
    nearer = jnp.roll(grid_field, 1, which_axis) + jnp.roll(grid_field, -1, which_axis)
    return -1.0 / 12.0 * outer + 4.0 / 3.0 * nearer - 2.5 * grid_field


def hamiltonian_apply(extended, local_potential):
    interior = extended[:, 2:-2]
    along_first = (
        -1.0 / 12.0 * (extended[:, :-4] + extended[:, 4:])
        + 4.0 / 3.0 * (extended[:, 1:-3] + extended[:, 3:-1])
        - 2.5 * interior
    )
    laplace = along_first + lap_periodic(interior, 2) + lap_periodic(interior, 3)
    return -0.5 * laplace + local_potential * interior


def shifted(extended, local_potential):
    return (hamiltonian_apply(extended, local_potential) - center * extended[:, 2:-2]) / halfwidth


def shifted_to(block, axis, shift):
    count = lax.axis_size(axis)
    return lax.ppermute(block, axis, [(i, (i + shift) % count) for i in range(count)])


def face_pieces(block, dim, axis, width):
    n = block.shape[dim]
    low, high = [], []
    for hop in range(1, -(-width // n) + 1):
        take = min(n, width - n * (hop - 1))
        low.insert(0, shifted_to(lax.slice_in_dim(block, n - take, None, axis=dim), axis, hop))
        high.append(shifted_to(lax.slice_in_dim(block, 0, take, axis=dim), axis, -hop))
    return low + [block] + high


def kernel_lap(field, which_axis):
    size = field.shape[which_axis]
    outer = pltpu.roll(field, 2, which_axis) + pltpu.roll(field, size - 2, which_axis)
    nearer = pltpu.roll(field, 1, which_axis) + pltpu.roll(field, size - 1, which_axis)
    return -1.0 / 12.0 * outer + 4.0 / 3.0 * nearer - 2.5 * field


def kernel_hamiltonian(extended, local_potential):
    interior = extended[:, 2:-2]
    along_first = (
        -1.0 / 12.0 * (extended[:, :-4] + extended[:, 4:])
        + 4.0 / 3.0 * (extended[:, 1:-3] + extended[:, 3:-1])
        - 2.5 * interior
    )
    laplace = along_first + kernel_lap(interior, 2) + kernel_lap(interior, 3)
    return -0.5 * laplace + local_potential[None] * interior


def kernel_shifted(extended, local_potential):
    return (kernel_hamiltonian(extended, local_potential) - center * extended[:, 2:-2]) / halfwidth


def kernel_stencil(planes, per_plane, outer_weight, near_weight):
    ny, nz = planes[0].shape[1], planes[0].shape[2]
    result = []
    for k in range(2, len(planes) - 2):
        here = planes[k]
        outer = (
            (planes[k - 2] + planes[k + 2])
            + (pltpu.roll(here, 2, 1) + pltpu.roll(here, ny - 2, 1))
            + (pltpu.roll(here, 2, 2) + pltpu.roll(here, nz - 2, 2))
        )
        nearer = (
            (planes[k - 1] + planes[k + 1])
            + (pltpu.roll(here, 1, 1) + pltpu.roll(here, ny - 1, 1))
            + (pltpu.roll(here, 1, 2) + pltpu.roll(here, nz - 1, 2))
        )
        result.append(outer_weight * outer + near_weight * nearer + per_plane[k - 2][None] * here)
    return result


def filter_kernel(*refs):
    *piece_refs, pot_ref, filtered_ref, applied_ref = refs
    wide = [r[:, k] for r in piece_refs for k in range(r.shape[1])]
    pot = pot_ref[...]
    outer_h, near_h = 0.5 / 12.0, -0.5 * 4.0 / 3.0
    diagonal_h = pot + 7.5 * 0.5
    diagonal_s = (diagonal_h - center) / halfwidth
    first_term = kernel_stencil(wide, diagonal_s, outer_h / halfwidth, near_h / halfwidth)
    second = kernel_stencil(first_term, 2.0 * diagonal_s[2:-2], 2.0 * outer_h / halfwidth, 2.0 * near_h / halfwidth)
    filtered_wide = [plane - psi_plane for plane, psi_plane in zip(second, wide[4:-4])]
    for k, plane in enumerate(filtered_wide[2:-2]):
        filtered_ref[:, k] = plane
    for k, plane in enumerate(kernel_stencil(filtered_wide, diagonal_h[4:-4], outer_h, near_h)):
        applied_ref[:, k] = plane


def filter_and_apply(pieces, pot_wide, group=8):
    bands, n = pieces[len(pieces) // 2].shape[:2]
    tail = pieces[0].shape[2:]

    def spec(planes):
        return pl.BlockSpec((group, planes) + tail, lambda i: (i, 0, 0, 0))

    out = jax.ShapeDtypeStruct((bands, n) + tail, jnp.float32)
    return pl.pallas_call(
        filter_kernel,
        grid=(bands // group,),
        in_specs=[spec(p.shape[1]) for p in pieces]
        + [pl.BlockSpec(pot_wide.shape, lambda i: (0, 0, 0))],
        out_specs=[spec(n), spec(n)],
        out_shape=[out, out],
        compiler_params=pltpu.CompilerParams(vmem_limit_bytes=48 * 1024 * 1024),
    )(*pieces, pot_wide)


def body(psi, potential, owner, stages=1):
    pot_wide = jnp.concatenate(face_pieces(potential, 0, "dom", 4), axis=0)
    owner_root = owner[0]
    step = psi.shape[0] // stages
    parts = []
    for stage in range(stages):
        block = lax.slice_in_dim(psi, stage * step, (stage + 1) * step, axis=0)
        filtered, applied = filter_and_apply(face_pieces(block, 1, "dom", 6), pot_wide)
        parts.append((filtered, applied, broadcast(filtered, "band", owner_root)))
    current, applied, owned_panel = (jnp.concatenate(p, axis=0) for p in zip(*parts))
    local_bands = current.shape[0]
    total_cells = current.shape[1] * current.shape[2] * current.shape[3] * lax.axis_size("dom")
    scale = 1.0 / total_cells
    flattened = current.reshape(local_bands, -1)
    panel_flat = owned_panel.reshape(local_bands, -1)
    ham_rows = jnp.einsum(
        "pc,bc->pb", panel_flat, applied.reshape(local_bands, -1), precision=lax.Precision.HIGHEST
    )
    over_rows = jnp.einsum("pc,bc->pb", panel_flat, flattened, precision=lax.Precision.HIGHEST)
    both = doubling_sum(jnp.stack([over_rows * scale, ham_rows * scale]), "dom")
    return (current, both[0], both[1])


def solution(mesh):
    placed = (P("band", "dom", None, None), P("dom", None, None), P())
    return jax.shard_map(
        body,
        mesh=mesh,
        in_specs=placed,
        out_specs=(P("band", "dom", None, None), P(None, "band"), P(None, "band")),
        check_vma=False,
    )
```

```python
import jax
import jax.numpy as jnp
from jax import lax
from jax.experimental import pallas as pl
from jax.experimental.pallas import tpu as pltpu
from jax.sharding import PartitionSpec as P


center = 4.9
halfwidth = 4.1


def broadcast(array, axis, root):
    count = lax.axis_size(axis)
    piece = array.shape[0] // count
    spread = lax.all_to_all(array, axis, 0, 0, tiled=True)
    mine = lax.dynamic_slice_in_dim(spread, root * piece, piece, 0)
    repeated = jnp.broadcast_to(mine[None], (count,) + mine.shape).reshape(array.shape)
    return lax.all_to_all(repeated, axis, 0, 0, tiled=True)


def doubling_sum(array, axis):
    count = lax.axis_size(axis)
    step = 1
    while step < count:
        array = array + lax.ppermute(array, axis, [(i, i ^ step) for i in range(count)])
        step *= 2
    return array


def lap_periodic(grid_field, which_axis):
    outer = jnp.roll(grid_field, 2, which_axis) + jnp.roll(grid_field, -2, which_axis)
    nearer = jnp.roll(grid_field, 1, which_axis) + jnp.roll(grid_field, -1, which_axis)
    return -1.0 / 12.0 * outer + 4.0 / 3.0 * nearer - 2.5 * grid_field


def hamiltonian_apply(extended, local_potential):
    interior = extended[:, 2:-2]
    along_first = (
        -1.0 / 12.0 * (extended[:, :-4] + extended[:, 4:])
        + 4.0 / 3.0 * (extended[:, 1:-3] + extended[:, 3:-1])
        - 2.5 * interior
    )
    laplace = along_first + lap_periodic(interior, 2) + lap_periodic(interior, 3)
    return -0.5 * laplace + local_potential * interior


def shifted(extended, local_potential):
    return (hamiltonian_apply(extended, local_potential) - center * extended[:, 2:-2]) / halfwidth


def shifted_to(block, axis, shift):
    count = lax.axis_size(axis)
    return lax.ppermute(block, axis, [(i, (i + shift) % count) for i in range(count)])


def face_pieces(block, dim, axis, width):
    n = block.shape[dim]
    low, high = [], []
    for hop in range(1, -(-width // n) + 1):
        take = min(n, width - n * (hop - 1))
        low.insert(0, shifted_to(lax.slice_in_dim(block, n - take, None, axis=dim), axis, hop))
        high.append(shifted_to(lax.slice_in_dim(block, 0, take, axis=dim), axis, -hop))
    return low + [block] + high


def kernel_lap(field, which_axis):
    size = field.shape[which_axis]
    outer = pltpu.roll(field, 2, which_axis) + pltpu.roll(field, size - 2, which_axis)
    nearer = pltpu.roll(field, 1, which_axis) + pltpu.roll(field, size - 1, which_axis)
    return -1.0 / 12.0 * outer + 4.0 / 3.0 * nearer - 2.5 * field


def kernel_hamiltonian(extended, local_potential):
    interior = extended[:, 2:-2]
    along_first = (
        -1.0 / 12.0 * (extended[:, :-4] + extended[:, 4:])
        + 4.0 / 3.0 * (extended[:, 1:-3] + extended[:, 3:-1])
        - 2.5 * interior
    )
    laplace = along_first + kernel_lap(interior, 2) + kernel_lap(interior, 3)
    return -0.5 * laplace + local_potential[None] * interior


def kernel_shifted(extended, local_potential):
    return (kernel_hamiltonian(extended, local_potential) - center * extended[:, 2:-2]) / halfwidth


def kernel_stencil(planes, per_plane, outer_weight, near_weight):
    ny, nz = planes[0].shape[1], planes[0].shape[2]
    result = []
    for k in range(2, len(planes) - 2):
        here = planes[k]
        outer = (
            (planes[k - 2] + planes[k + 2])
            + (pltpu.roll(here, 2, 1) + pltpu.roll(here, ny - 2, 1))
            + (pltpu.roll(here, 2, 2) + pltpu.roll(here, nz - 2, 2))
        )
        nearer = (
            (planes[k - 1] + planes[k + 1])
            + (pltpu.roll(here, 1, 1) + pltpu.roll(here, ny - 1, 1))
            + (pltpu.roll(here, 1, 2) + pltpu.roll(here, nz - 1, 2))
        )
        result.append(outer_weight * outer + near_weight * nearer + per_plane[k - 2][None] * here)
    return result


def filter_kernel(*refs):
    *piece_refs, pot_ref, filtered_ref, stacked_ref = refs
    wide = [r[:, k] for r in piece_refs for k in range(r.shape[1])]
    pot = pot_ref[...]
    outer_h, near_h = 0.5 / 12.0, -0.5 * 4.0 / 3.0
    diagonal_h = pot + 7.5 * 0.5
    diagonal_s = (diagonal_h - center) / halfwidth
    first_term = kernel_stencil(wide, diagonal_s, outer_h / halfwidth, near_h / halfwidth)
    second = kernel_stencil(first_term, 2.0 * diagonal_s[2:-2], 2.0 * outer_h / halfwidth, 2.0 * near_h / halfwidth)
    filtered_wide = [plane - psi_plane for plane, psi_plane in zip(second, wide[4:-4])]
    for k, plane in enumerate(filtered_wide[2:-2]):
        filtered_ref[:, k] = plane
        stacked_ref[0, :, k] = plane
    for k, plane in enumerate(kernel_stencil(filtered_wide, diagonal_h[4:-4], outer_h, near_h)):
        stacked_ref[1, :, k] = plane


def filter_and_apply(pieces, pot_wide, group=8):
    bands, n = pieces[len(pieces) // 2].shape[:2]
    tail = pieces[0].shape[2:]

    def spec(planes):
        return pl.BlockSpec((group, planes) + tail, lambda i: (i, 0, 0, 0))

    return pl.pallas_call(
        filter_kernel,
        grid=(bands // group,),
        in_specs=[spec(p.shape[1]) for p in pieces]
        + [pl.BlockSpec(pot_wide.shape, lambda i: (0, 0, 0))],
        out_specs=[spec(n), pl.BlockSpec((2, group, n) + tail, lambda i: (0, i, 0, 0, 0))],
        out_shape=[
            jax.ShapeDtypeStruct((bands, n) + tail, jnp.float32),
            jax.ShapeDtypeStruct((2, bands, n) + tail, jnp.float32),
        ],
        compiler_params=pltpu.CompilerParams(vmem_limit_bytes=48 * 1024 * 1024),
    )(*pieces, pot_wide)


def body(psi, potential, owner, stages=1):
    pot_wide = jnp.concatenate(face_pieces(potential, 0, "dom", 4), axis=0)
    owner_root = owner[0]
    step = psi.shape[0] // stages
    parts = []
    for stage in range(stages):
        block = lax.slice_in_dim(psi, stage * step, (stage + 1) * step, axis=0)
        filtered, stacked = filter_and_apply(face_pieces(block, 1, "dom", 6), pot_wide)
        parts.append((filtered, stacked, broadcast(filtered, "band", owner_root)))
    current, stacked, owned_panel = (jnp.concatenate(p, axis=int(i == 1)) for i, p in enumerate(zip(*parts)))
    local_bands = current.shape[0]
    total_cells = current.shape[1] * current.shape[2] * current.shape[3] * lax.axis_size("dom")
    scale = 1.0 / total_cells
    panel_flat = owned_panel.reshape(local_bands, -1)
    rows = jnp.einsum(
        "pc,bc->pb", panel_flat, stacked.reshape(2 * local_bands, -1), precision=lax.Precision.HIGHEST
    )
    over_rows, ham_rows = rows[:, :local_bands], rows[:, local_bands:]
    both = doubling_sum(jnp.stack([over_rows * scale, ham_rows * scale]), "dom")
    return (current, both[0], both[1])


def solution(mesh):
    placed = (P("band", "dom", None, None), P("dom", None, None), P())
    return jax.shard_map(
        body,
        mesh=mesh,
        in_specs=placed,
        out_specs=(P("band", "dom", None, None), P(None, "band"), P(None, "band")),
        check_vma=False,
    )
```

```python
import jax
import jax.numpy as jnp
from jax import lax
from jax.experimental import pallas as pl
from jax.experimental.pallas import tpu as pltpu
from jax.sharding import PartitionSpec as P


center = 4.9
halfwidth = 4.1


def broadcast(array, axis, root):
    count = lax.axis_size(axis)
    piece = array.shape[0] // count
    spread = lax.all_to_all(array, axis, 0, 0, tiled=True)
    mine = lax.dynamic_slice_in_dim(spread, root * piece, piece, 0)
    repeated = jnp.broadcast_to(mine[None], (count,) + mine.shape).reshape(array.shape)
    return lax.all_to_all(repeated, axis, 0, 0, tiled=True)


def doubling_sum(array, axis):
    count = lax.axis_size(axis)
    step = 1
    while step < count:
        array = array + lax.ppermute(array, axis, [(i, i ^ step) for i in range(count)])
        step *= 2
    return array


def lap_periodic(grid_field, which_axis):
    outer = jnp.roll(grid_field, 2, which_axis) + jnp.roll(grid_field, -2, which_axis)
    nearer = jnp.roll(grid_field, 1, which_axis) + jnp.roll(grid_field, -1, which_axis)
    return -1.0 / 12.0 * outer + 4.0 / 3.0 * nearer - 2.5 * grid_field


def hamiltonian_apply(extended, local_potential):
    interior = extended[:, 2:-2]
    along_first = (
        -1.0 / 12.0 * (extended[:, :-4] + extended[:, 4:])
        + 4.0 / 3.0 * (extended[:, 1:-3] + extended[:, 3:-1])
        - 2.5 * interior
    )
    laplace = along_first + lap_periodic(interior, 2) + lap_periodic(interior, 3)
    return -0.5 * laplace + local_potential * interior


def shifted(extended, local_potential):
    return (hamiltonian_apply(extended, local_potential) - center * extended[:, 2:-2]) / halfwidth


def shifted_to(block, axis, shift):
    count = lax.axis_size(axis)
    return lax.ppermute(block, axis, [(i, (i + shift) % count) for i in range(count)])


def face_pieces(block, dim, axis, width):
    n = block.shape[dim]
    low, high = [], []
    for hop in range(1, -(-width // n) + 1):
        take = min(n, width - n * (hop - 1))
        low.insert(0, shifted_to(lax.slice_in_dim(block, n - take, None, axis=dim), axis, hop))
        high.append(shifted_to(lax.slice_in_dim(block, 0, take, axis=dim), axis, -hop))
    return low + [block] + high


def kernel_lap(field, which_axis):
    size = field.shape[which_axis]
    outer = pltpu.roll(field, 2, which_axis) + pltpu.roll(field, size - 2, which_axis)
    nearer = pltpu.roll(field, 1, which_axis) + pltpu.roll(field, size - 1, which_axis)
    return -1.0 / 12.0 * outer + 4.0 / 3.0 * nearer - 2.5 * field


def kernel_hamiltonian(extended, local_potential):
    interior = extended[:, 2:-2]
    along_first = (
        -1.0 / 12.0 * (extended[:, :-4] + extended[:, 4:])
        + 4.0 / 3.0 * (extended[:, 1:-3] + extended[:, 3:-1])
        - 2.5 * interior
    )
    laplace = along_first + kernel_lap(interior, 2) + kernel_lap(interior, 3)
    return -0.5 * laplace + local_potential[None] * interior


def kernel_shifted(extended, local_potential):
    return (kernel_hamiltonian(extended, local_potential) - center * extended[:, 2:-2]) / halfwidth


def kernel_stencil(planes, per_plane, outer_weight, near_weight):
    ny, nz = planes[0].shape[1], planes[0].shape[2]
    result = []
    for k in range(2, len(planes) - 2):
        here = planes[k]
        outer = (
            (planes[k - 2] + planes[k + 2])
            + (pltpu.roll(here, 2, 1) + pltpu.roll(here, ny - 2, 1))
            + (pltpu.roll(here, 2, 2) + pltpu.roll(here, nz - 2, 2))
        )
        nearer = (
            (planes[k - 1] + planes[k + 1])
            + (pltpu.roll(here, 1, 1) + pltpu.roll(here, ny - 1, 1))
            + (pltpu.roll(here, 1, 2) + pltpu.roll(here, nz - 1, 2))
        )
        result.append(outer_weight * outer + near_weight * nearer + per_plane[k - 2][None] * here)
    return result


def filter_kernel(*refs):
    *piece_refs, pot_ref, filtered_ref, stacked_ref = refs
    wide = [r[:, k] for r in piece_refs for k in range(r.shape[1])]
    pot = pot_ref[...]
    outer_h, near_h = 0.5 / 12.0, -0.5 * 4.0 / 3.0
    diagonal_h = pot + 7.5 * 0.5
    diagonal_s = (diagonal_h - center) / halfwidth
    first_term = kernel_stencil(wide, diagonal_s, outer_h / halfwidth, near_h / halfwidth)
    second = kernel_stencil(first_term, 2.0 * diagonal_s[2:-2], 2.0 * outer_h / halfwidth, 2.0 * near_h / halfwidth)
    filtered_wide = [plane - psi_plane for plane, psi_plane in zip(second, wide[4:-4])]
    for k, plane in enumerate(filtered_wide[2:-2]):
        filtered_ref[:, k] = plane
        stacked_ref[0, :, k] = plane
    for k, plane in enumerate(kernel_stencil(filtered_wide, diagonal_h[4:-4], outer_h, near_h)):
        stacked_ref[1, :, k] = plane


def filter_and_apply(pieces, pot_wide, group=8):
    bands, n = pieces[len(pieces) // 2].shape[:2]
    tail = pieces[0].shape[2:]

    def spec(planes):
        return pl.BlockSpec((group, planes) + tail, lambda i: (i, 0, 0, 0))

    return pl.pallas_call(
        filter_kernel,
        grid=(bands // group,),
        in_specs=[spec(p.shape[1]) for p in pieces]
        + [pl.BlockSpec(pot_wide.shape, lambda i: (0, 0, 0))],
        out_specs=[spec(n), pl.BlockSpec((2, group, n) + tail, lambda i: (0, i, 0, 0, 0))],
        out_shape=[
            jax.ShapeDtypeStruct((bands, n) + tail, jnp.float32),
            jax.ShapeDtypeStruct((2, bands, n) + tail, jnp.float32),
        ],
        compiler_params=pltpu.CompilerParams(vmem_limit_bytes=48 * 1024 * 1024),
    )(*pieces, pot_wide)


def body(psi, potential, owner, stages=1):
    pot_wide = jnp.concatenate(face_pieces(potential, 0, "dom", 4), axis=0)
    owner_root = owner[0]
    step = psi.shape[0] // stages
    parts = []
    for stage in range(stages):
        block = lax.slice_in_dim(psi, stage * step, (stage + 1) * step, axis=0)
        filtered, stacked = filter_and_apply(face_pieces(block, 1, "dom", 6), pot_wide)
        parts.append((filtered, stacked, broadcast(filtered, "band", owner_root)))
    current, stacked, owned_panel = (jnp.concatenate(p, axis=int(i == 1)) for i, p in enumerate(zip(*parts)))
    local_bands = current.shape[0]
    total_cells = current.shape[1] * current.shape[2] * current.shape[3] * lax.axis_size("dom")
    scale = 1.0 / total_cells
    panel_flat = owned_panel.reshape(local_bands, -1)
    rows = jnp.einsum(
        "pc,kbc->kpb", panel_flat, stacked.reshape(2, local_bands, -1), precision=lax.Precision.HIGHEST
    )
    both = doubling_sum(rows * scale, "dom")
    return (current, both[0], both[1])


def solution(mesh):
    placed = (P("band", "dom", None, None), P("dom", None, None), P())
    return jax.shard_map(
        body,
        mesh=mesh,
        in_specs=placed,
        out_specs=(P("band", "dom", None, None), P(None, "band"), P(None, "band")),
        check_vma=False,
    )
```
